256 devices in a mesh: row: 32 (over x, z_hi, y), col: 8 (over z_lo, core).
Axes of the slice: x: 4, y: 4, z: 8 (z_hi: 2, z_lo: 4; z = z_hi * 4 + z_lo), core: 2. Of those that a mesh axis runs over, the one named last changes fastest.
Arguments:
- tile_values: bfloat16 [32, 8, 256, 128, 128], P('row', 'col'), may hold values from -0.125 to 0.125
- tile_coords: int32 [32, 8, 2, 256], P('row', 'col'), may hold values from 0 to 63, as said below
- tile_counts: int32 [32, 8], P('row', 'col'), may hold values from 32 to 256, as said below
- features: bfloat16 [8, 32, 256, 256], P('col', 'row'), may hold values from -6 to 6
- weight_matrix: bfloat16 [256, 256], replicated, may hold values from -0.375 to 0.375
- out_grad: bfloat16 [32, 8, 256, 256], P('row', 'col'), may hold values from -6 to 6
Outputs:
- activated: bfloat16 [32, 8, 256, 256], P('row', 'col')
- feature_grad: float32 [8, 32, 256, 256], P('col', 'row')
- weight_grad: float32 [256, 256], replicated
The draws below stay inside these ranges and needn't reach their ends.
Inputs may be any that keep to these rules, and one draw needn't show every extreme that they name: `tile_coords`: each device's 256 slots name distinct tile positions; the tile row is below 16. `tile_counts`: some device has all 256 slots live.
All inputs are finite; a program needn't handle non-finite values.
Results may differ from the reference program's by a relative error of at most 0.015.
Values may be sent and summed in bfloat16 or wider, within the bound.
No kernel may reach another device: no remote copies, remote signals or barrier semaphores. Data moves between devices by JAX's collectives and lax.ppermute only.
A program may use at most 128 MiB of HBM per device.

```python
import jax
import jax.numpy as jnp
from jax import lax

F = 256
TILE = 128
TPR = 16
SUB = 256
TROWS = 16
TCOLS = 64
TMAX = 256
N_ROW = 32
N_COL = 8


def draw_tile_coords(key, part):
    keys = jax.random.split(key, N_ROW * N_COL)

    def one_device(device_key):
        order = jax.random.permutation(device_key, TROWS * TCOLS)[:TMAX].astype(jnp.int32)
        return jnp.stack([order // TCOLS, order % TCOLS])
    return jax.vmap(one_device)(keys).reshape(N_ROW, N_COL, 2, TMAX)


def draw_tile_counts(key, part):
    key_shift, key_full = jax.random.split(jax.random.fold_in(key, 7))
    shifts = jax.random.randint(key_shift, (N_ROW * N_COL,), 0, 4)
    full_device = jax.random.randint(key_full, (), 0, N_ROW * N_COL)
    shifts = jnp.where(jnp.arange(N_ROW * N_COL) == full_device, 0, shifts)
    counts = jnp.right_shift(jnp.full((N_ROW * N_COL,), TMAX, jnp.int32), shifts.astype(jnp.int32))
    return counts.reshape(N_ROW, N_COL).astype(jnp.int32)


def levels(own_key, shape, cuts, low, high):
    factor_of, own = 1.0, jax.random.fold_in(own_key, 6)
    for position, blocks in cuts:
        draws = jnp.exp(jax.random.uniform(jax.random.fold_in(own, position), (blocks,), jnp.float32, low / len(cuts), high / len(cuts)))
        factor_of = factor_of * jnp.repeat(draws, shape[position] // blocks).reshape([-1 if axis == position else 1 for axis in range(len(shape))])
    return factor_of


def centred(own_key, dims, spread, reach, cuts=(), kind=jnp.bfloat16):
    entries = jax.random.normal(own_key, dims, jnp.float32) * spread
    if len(cuts) > 0:
        entries = levels(own_key, dims, cuts, -0.22, 0.18) * entries
    return jnp.clip(entries, min=-reach, max=reach).astype(kind)


def setup_inputs(seed: int = 0) -> dict:
    splits = jax.random.split(jax.random.key(seed), 7)
    return {
        "tile_values": centred(splits[0], (N_ROW, N_COL, TMAX, TILE, TILE), (1.0 / (TPR * TILE * N_COL) ** 0.5), 0.125, ((0, 32), (1, 8))),
        "tile_coords": draw_tile_coords(jax.random.fold_in(splits[6], 71), 0),
        "tile_counts": draw_tile_counts(jax.random.fold_in(splits[6], 71), 0),
        "features": centred(splits[3], (N_COL, N_ROW, SUB, F), 1.0, 6.0, ((0, 8), (1, 32))),
        "weight_matrix": centred(splits[4], (F, F), F ** -0.5, 0.375),
        "out_grad": centred(splits[5], (N_ROW, N_COL, SUB, F), 1.0, 6.0, ((0, 32), (1, 8))),
    }


def reference(tile_values, tile_coords, tile_counts, features, weight_matrix, out_grad):
    n_row = tile_counts.shape[0]
    n_col = tile_counts.shape[1]
    tile_side = tile_values.shape[-1]
    width = features.shape[-1]
    sub_rows = features.shape[2]
    row_tiles = n_col * sub_rows // tile_side
    col_tiles = n_row * sub_rows // tile_side
    slot_ids = jnp.arange(tile_values.shape[2], dtype=jnp.int32)

    def forward_block(rowid):
        def one_col(totals, colid):
            source = features[colid].reshape(col_tiles, tile_side, width).astype(jnp.float32)
            values = tile_values[rowid, colid].astype(jnp.float32)
            picked = source[tile_coords[rowid, colid, 1]]
            products = jnp.einsum("kij,kjf->kif", values, picked, precision=lax.Precision.HIGHEST)
            is_live = slot_ids < tile_counts[rowid, colid]
            products = jnp.where(is_live[:, None, None], products, 0.0)
            return totals + jax.ops.segment_sum(products, tile_coords[rowid, colid, 0], num_segments=row_tiles), None
        totals, _ = lax.scan(one_col, jnp.zeros((row_tiles, tile_side, width), jnp.float32), jnp.arange(n_col, dtype=jnp.int32))
        return totals

    mixed = lax.map(forward_block, jnp.arange(n_row, dtype=jnp.int32)).astype(jnp.bfloat16)
    flat = mixed.reshape(-1, width)
    pre = jnp.dot(flat, weight_matrix, preferred_element_type=jnp.float32)
    sigma = jax.nn.sigmoid(pre)
    activated = (pre * sigma).astype(jnp.bfloat16)
    pre_grad = (out_grad.reshape(-1, width).astype(jnp.float32) * sigma * (1.0 + pre * (1.0 - sigma))).astype(jnp.bfloat16)
    weight_grad = jnp.dot(flat.T, pre_grad, preferred_element_type=jnp.float32)
    mixed_grad = jnp.dot(pre_grad, weight_matrix.T, preferred_element_type=jnp.float32).astype(jnp.bfloat16)
    mixed_grad = mixed_grad.reshape(n_row, row_tiles, tile_side, width)

    def backward_block(colid):
        def one_row(totals, rowid):
            source = mixed_grad[rowid].astype(jnp.float32)
            values = tile_values[rowid, colid].astype(jnp.float32)
            picked = source[tile_coords[rowid, colid, 0]]
            products = jnp.einsum("kij,kif->kjf", values, picked, precision=lax.Precision.HIGHEST)
            is_live = slot_ids < tile_counts[rowid, colid]
            products = jnp.where(is_live[:, None, None], products, 0.0)
            return totals + jax.ops.segment_sum(products, tile_coords[rowid, colid, 1], num_segments=col_tiles), None
        totals, _ = lax.scan(one_row, jnp.zeros((col_tiles, tile_side, width), jnp.float32), jnp.arange(n_row, dtype=jnp.int32))
        return totals

    feature_grad = lax.map(backward_block, jnp.arange(n_col, dtype=jnp.int32))
    feature_grad = feature_grad.reshape(n_col, n_row, sub_rows, width)
    return activated.reshape(n_row, n_col, sub_rows, width), feature_grad, weight_grad
```

```python
import math

import jax
import jax.numpy as jnp
from jax import lax
from jax.sharding import PartitionSpec as P


def aggregate(values, pick_index, place_index, live_count, source, segments, transposed):
    slot_total = values.shape[0]
    block_size = math.gcd(slot_total, 32)
    tile_side = values.shape[1]
    width = source.shape[2]

    def block_step(block, totals):
        offset = block * block_size
        chosen = lax.dynamic_slice_in_dim(values, offset, block_size, 0)
        picks = lax.dynamic_slice_in_dim(pick_index, offset, block_size, 0)
        places = lax.dynamic_slice_in_dim(place_index, offset, block_size, 0)
        picked = source[picks]
        if transposed:
            products = jnp.einsum(
                "kij,kif->kjf", chosen, picked, preferred_element_type=jnp.float32
            )
        else:
            products = jnp.einsum(
                "kij,kjf->kif", chosen, picked, preferred_element_type=jnp.float32
            )
        is_live = offset + jnp.arange(block_size, dtype=jnp.int32) < live_count
        products = jnp.where(is_live[:, None, None], products, 0.0)
        return totals.at[places].add(products)

    start_totals = jnp.zeros((segments, tile_side, width), jnp.float32)
    upper = (live_count + block_size - 1) // block_size
    return lax.fori_loop(0, upper, block_step, start_totals)


def scatter_sum(partial, axis_name):
    received = lax.all_to_all(partial, axis_name, 0, 0, tiled=True)
    return jnp.sum(received.astype(jnp.float32), axis=0)


def all_sum(terms):
    axes = ("row", "col")
    count = lax.axis_size("row") * lax.axis_size("col")
    rows, width = terms.shape
    pieces = terms.reshape(count, rows // count, width)
    mine = jnp.sum(lax.all_to_all(pieces, axes, 0, 0, tiled=True), axis=0, keepdims=True)
    spread = jnp.broadcast_to(mine, (count, rows // count, width))
    return lax.all_to_all(spread, axes, 0, 0, tiled=True).reshape(rows, width)


def shards(tile_values, tile_coords, tile_counts, features, weight_matrix, out_grad):
    values = tile_values[0, 0]
    coords = tile_coords[0, 0]
    live_count = tile_counts[0, 0]
    tile_side = values.shape[1]
    sub_rows = features.shape[2]
    width = features.shape[3]
    n_col = lax.axis_size("col")
    n_row = lax.axis_size("row")
    row_tiles = n_col * sub_rows // tile_side
    column_block = lax.all_gather(features, "row", axis=1, tiled=True)
    col_source = column_block.reshape(-1, tile_side, width)
    col_tiles = col_source.shape[0]
    partial_value = aggregate(
        values, coords[1], coords[0], live_count, col_source, row_tiles, False
    )
    partial_value = partial_value.reshape(n_col, sub_rows, width)
    share = scatter_sum(partial_value, "col")
    mixed = share.astype(jnp.bfloat16).reshape(sub_rows, width)
    pre = jnp.dot(mixed, weight_matrix, preferred_element_type=jnp.float32)
    sigma = jax.nn.sigmoid(pre)
    activated = (pre * sigma).astype(jnp.bfloat16)
    pre_grad = (
        out_grad.reshape(sub_rows, width).astype(jnp.float32) * sigma * (1.0 + pre * (1.0 - sigma))
    ).astype(jnp.bfloat16)
    weight_terms = jnp.dot(mixed.T, pre_grad, preferred_element_type=jnp.float32)
    own_grad = jnp.dot(pre_grad, weight_matrix.T, preferred_element_type=jnp.float32).astype(
        jnp.bfloat16
    )
    mixed_grad = lax.all_gather(own_grad.reshape(1, 1, sub_rows, width), "col", axis=1, tiled=True)
    weight_grad = all_sum(weight_terms)
    row_source = mixed_grad.reshape(row_tiles, tile_side, width)
    back_partial = aggregate(values, coords[0], coords[1], live_count, row_source, col_tiles, True)
    back_partial = back_partial.reshape(n_row, sub_rows, width).astype(jnp.bfloat16)
    feature_grad = scatter_sum(back_partial, "row").reshape(1, 1, sub_rows, width)
    return (activated.reshape(1, 1, sub_rows, width), feature_grad, weight_grad)


def solution(mesh):
    return jax.shard_map(
        shards,
        mesh=mesh,
        in_specs=(
            P("row", "col", None, None, None),
            P("row", "col", None, None),
            P("row", "col"),
            P("col", "row", None, None),
            P(),
            P("row", "col", None, None),
        ),
        out_specs=(P("row", "col", None, None), P("col", "row", None, None), P()),
        check_vma=False,
    )
```

```python
import jax
import jax.numpy as jnp
from jax import lax
from jax.experimental import pallas as pl
from jax.experimental.pallas import tpu as pltpu
from jax.sharding import PartitionSpec as P

GROUP = 32


def tile_aggregate(values, pick_index, place_index, live_count, source, segments, transposed, out_dtype):
    slot_total, tile_side, _ = values.shape
    width = source.shape[2]
    steps = slot_total // GROUP

    def kernel(picks_ref, places_ref, count_ref, vals_ref, src_ref, out_ref, acc_ref):
        step = pl.program_id(0)

        @pl.when(step == 0)
        def _():
            acc_ref[...] = jnp.zeros_like(acc_ref)

        def slot(j, carry):
            k = step * GROUP + j

            @pl.when(k < count_ref[0])
            def _():
                src_tile = src_ref[picks_ref[k]]
                tile = vals_ref[j]
                if transposed:
                    term = lax.dot_general(tile, src_tile, (((0,), (0,)), ((), ())),
                                           preferred_element_type=jnp.float32)
                else:
                    term = jnp.dot(tile, src_tile, preferred_element_type=jnp.float32)
                place = places_ref[k]
                acc_ref[place] += term

            return carry

        lax.fori_loop(0, GROUP, slot, 0)

        @pl.when(step == steps - 1)
        def _():
            out_ref[...] = acc_ref[...].astype(out_ref.dtype)

    def vals_map(i, picks, places, count):
        return (jnp.minimum(i, (count[0] - 1) // GROUP), 0, 0)

    grid_spec = pltpu.PrefetchScalarGridSpec(
        num_scalar_prefetch=3,
        grid=(steps,),
        in_specs=[
            pl.BlockSpec((GROUP, tile_side, tile_side), vals_map),
            pl.BlockSpec(source.shape, lambda i, *_: (0, 0, 0)),
        ],
        out_specs=pl.BlockSpec((segments, tile_side, width), lambda i, *_: (0, 0, 0)),
        scratch_shapes=[pltpu.VMEM((segments, tile_side, width), jnp.float32)],
    )
    flops = 2 * slot_total * tile_side * tile_side * width
    return pl.pallas_call(
        kernel,
        grid_spec=grid_spec,
        out_shape=jax.ShapeDtypeStruct((segments, tile_side, width), out_dtype),
        compiler_params=pltpu.CompilerParams(
            dimension_semantics=("arbitrary",), vmem_limit_bytes=48 * 1024 * 1024
        ),
        cost_estimate=pl.CostEstimate(
            flops=flops, transcendentals=0,
            bytes_accessed=values.size * 2 + source.size * 2 + segments * tile_side * width * jnp.dtype(out_dtype).itemsize,
        ),
    )(pick_index, place_index, live_count.reshape(1), values, source)


def scatter_sum(partial, axis_name):
    received = lax.all_to_all(partial, axis_name, 0, 0, tiled=True)
    return jnp.sum(received.astype(jnp.float32), axis=0)


def all_sum(terms):
    axes = ("row", "col")
    count = lax.axis_size("row") * lax.axis_size("col")
    rows, width = terms.shape
    pieces = terms.reshape(count, rows // count, width)
    mine = jnp.sum(lax.all_to_all(pieces, axes, 0, 0, tiled=True), axis=0, keepdims=True)
    spread = jnp.broadcast_to(mine, (count, rows // count, width))
    return lax.all_to_all(spread, axes, 0, 0, tiled=True).reshape(rows, width)


def shards(tile_values, tile_coords, tile_counts, features, weight_matrix, out_grad):
    values = tile_values[0, 0]
    coords = tile_coords[0, 0]
    live_count = tile_counts[0, 0]
    tile_side = values.shape[1]
    sub_rows = features.shape[2]
    width = features.shape[3]
    n_col = lax.axis_size("col")
    n_row = lax.axis_size("row")
    row_tiles = n_col * sub_rows // tile_side
    column_block = lax.all_gather(features, "row", axis=1, tiled=True)
    col_source = column_block.reshape(-1, tile_side, width)
    col_tiles = col_source.shape[0]
    partial_value = tile_aggregate(
        values, coords[1], coords[0], live_count, col_source, row_tiles, False, jnp.float32
    )
    partial_value = partial_value.reshape(n_col, sub_rows, width)
    share = scatter_sum(partial_value, "col")
    mixed = share.astype(jnp.bfloat16).reshape(sub_rows, width)
    pre = jnp.dot(mixed, weight_matrix, preferred_element_type=jnp.float32)
    sigma = jax.nn.sigmoid(pre)
    activated = (pre * sigma).astype(jnp.bfloat16)
    pre_grad = (
        out_grad.reshape(sub_rows, width).astype(jnp.float32) * sigma * (1.0 + pre * (1.0 - sigma))
    ).astype(jnp.bfloat16)
    weight_terms = jnp.dot(mixed.T, pre_grad, preferred_element_type=jnp.float32)
    own_grad = jnp.dot(pre_grad, weight_matrix.T, preferred_element_type=jnp.float32).astype(
        jnp.bfloat16
    )
    mixed_grad = lax.all_gather(own_grad.reshape(1, 1, sub_rows, width), "col", axis=1, tiled=True)
    weight_grad = all_sum(weight_terms)
    row_source = mixed_grad.reshape(row_tiles, tile_side, width)
    back_partial = tile_aggregate(
        values, coords[0], coords[1], live_count, row_source, col_tiles, True, jnp.bfloat16
    )
    back_partial = back_partial.reshape(n_row, sub_rows, width)
    feature_grad = scatter_sum(back_partial, "row").reshape(1, 1, sub_rows, width)
    return (activated.reshape(1, 1, sub_rows, width), feature_grad, weight_grad)


def solution(mesh):
    return jax.shard_map(
        shards,
        mesh=mesh,
        in_specs=(
            P("row", "col", None, None, None),
            P("row", "col", None, None),
            P("row", "col"),
            P("col", "row", None, None),
            P(),
            P("row", "col", None, None),
        ),
        out_specs=(P("row", "col", None, None), P("col", "row", None, None), P()),
        check_vma=False,
    )
```

```python
import jax
import jax.numpy as jnp
from jax import lax
from jax.experimental import pallas as pl
from jax.experimental.pallas import tpu as pltpu
from jax.sharding import PartitionSpec as P

GROUP = 32


def tile_aggregate(values, pick_index, place_index, live_count, source, segments, transposed, out_dtype):
    slot_total, tile_side, _ = values.shape
    width = source.shape[2]
    steps = slot_total // GROUP

    def kernel(picks_ref, places_ref, count_ref, vals_ref, src_ref, out_ref, acc_ref):
        step = pl.program_id(0)

        @pl.when(step == 0)
        def _():
            acc_ref[...] = jnp.zeros_like(acc_ref)

        def slot(j, carry):
            k = step * GROUP + j

            @pl.when(k < count_ref[0])
            def _():
                src_tile = src_ref[picks_ref[k]]
                tile = vals_ref[j]
                if transposed:
                    term = lax.dot_general(tile, src_tile, (((0,), (0,)), ((), ())),
                                           preferred_element_type=jnp.float32)
                else:
                    term = jnp.dot(tile, src_tile, preferred_element_type=jnp.float32)
                place = places_ref[k]
                acc_ref[place] += term

            return carry

        lax.fori_loop(0, GROUP, slot, 0)

        @pl.when(step == steps - 1)
        def _():
            out_ref[...] = acc_ref[...].astype(out_ref.dtype)

    def vals_map(i, picks, places, count):
        return (jnp.minimum(i, (count[0] - 1) // GROUP), 0, 0)

    grid_spec = pltpu.PrefetchScalarGridSpec(
        num_scalar_prefetch=3,
        grid=(steps,),
        in_specs=[
            pl.BlockSpec((GROUP, tile_side, tile_side), vals_map),
            pl.BlockSpec(source.shape, lambda i, *_: (0, 0, 0)),
        ],
        out_specs=pl.BlockSpec((segments, tile_side, width), lambda i, *_: (0, 0, 0)),
        scratch_shapes=[pltpu.VMEM((segments, tile_side, width), jnp.float32)],
    )
    flops = 2 * slot_total * tile_side * tile_side * width
    return pl.pallas_call(
        kernel,
        grid_spec=grid_spec,
        out_shape=jax.ShapeDtypeStruct((segments, tile_side, width), out_dtype),
        compiler_params=pltpu.CompilerParams(
            dimension_semantics=("arbitrary",), vmem_limit_bytes=48 * 1024 * 1024
        ),
        cost_estimate=pl.CostEstimate(
            flops=flops, transcendentals=0,
            bytes_accessed=values.size * 2 + source.size * 2 + segments * tile_side * width * jnp.dtype(out_dtype).itemsize,
        ),
    )(pick_index, place_index, live_count.reshape(1), values, source)


def scatter_sum(partial, axis_name):
    received = lax.all_to_all(partial, axis_name, 0, 0, tiled=True)
    return jnp.sum(received.astype(jnp.float32), axis=0)


def ring_step_pairs(size, stride, digits, shift):
    pairs = []
    for index in range(size):
        digit = (index // stride) % digits
        pairs.append((index, index + (((digit + shift) % digits) - digit) * stride))
    return pairs


def ring_reduce(partial, axis_name, stride, link_dtype):
    digits = partial.shape[0]
    size = lax.axis_size(axis_name)
    digit = (lax.axis_index(axis_name) // stride) % digits
    half = partial.shape[1] // 2
    lead = partial.shape[1]

    def block(offset):
        return lax.dynamic_index_in_dim(partial, (digit + offset) % digits, 0, keepdims=False)

    rightward = ring_step_pairs(size, stride, digits, 1)
    leftward = ring_step_pairs(size, stride, digits, -1)
    far = block(2)
    to_right = jnp.concatenate([block(1), far[:half]]).astype(link_dtype)
    to_left = jnp.concatenate([block(digits - 1), far[half:]]).astype(link_dtype)
    from_left = lax.ppermute(to_right, axis_name, rightward)
    from_right = lax.ppermute(to_left, axis_name, leftward)
    relay_left = lax.ppermute(from_left[lead:], axis_name, rightward)
    relay_right = lax.ppermute(from_right[lead:], axis_name, leftward)
    total = block(0).astype(jnp.float32) + from_left[:lead].astype(jnp.float32)
    total = total + from_right[:lead].astype(jnp.float32)
    return total + jnp.concatenate([relay_left, relay_right]).astype(jnp.float32)


def pair_reduce(partial, axis_name, stride, link_dtype):
    size = lax.axis_size(axis_name)
    digit = (lax.axis_index(axis_name) // stride) % 2
    pairs = [(index, index ^ stride) for index in range(size)]
    mine = lax.dynamic_index_in_dim(partial, digit, 0, keepdims=False)
    other = lax.dynamic_index_in_dim(partial, 1 - digit, 0, keepdims=False)
    return mine.astype(jnp.float32) + lax.ppermute(other.astype(link_dtype), axis_name, pairs).astype(jnp.float32)


def row_reduce(partial, link_dtype):
    count, rows, width = partial.shape
    split = width // 2
    first = partial[:, :, :split].reshape(4, 8, rows, split)
    first = ring_reduce(first, "row", 8, link_dtype).reshape(2, 4, rows, split)
    first = jnp.swapaxes(first, 0, 1)
    first = ring_reduce(first, "row", 1, link_dtype)
    second = partial[:, :, split:].reshape(4, 2, 4, rows, split)
    second = jnp.transpose(second, (2, 0, 1, 3, 4))
    second = ring_reduce(second, "row", 1, link_dtype).reshape(4, 2, rows, split)
    second = ring_reduce(second, "row", 8, link_dtype)
    both = jnp.concatenate([first, second], axis=-1)
    return pair_reduce(both, "row", 4, link_dtype)


def all_sum(terms):
    axes = ("row", "col")
    count = lax.axis_size("row") * lax.axis_size("col")
    rows, width = terms.shape
    pieces = terms.reshape(count, rows // count, width)
    mine = jnp.sum(lax.all_to_all(pieces, axes, 0, 0, tiled=True), axis=0, keepdims=True)
    spread = jnp.broadcast_to(mine, (count, rows // count, width))
    return lax.all_to_all(spread, axes, 0, 0, tiled=True).reshape(rows, width)


def shards(tile_values, tile_coords, tile_counts, features, weight_matrix, out_grad):
    values = tile_values[0, 0]
    coords = tile_coords[0, 0]
    live_count = tile_counts[0, 0]
    tile_side = values.shape[1]
    sub_rows = features.shape[2]
    width = features.shape[3]
    n_col = lax.axis_size("col")
    n_row = lax.axis_size("row")
    row_tiles = n_col * sub_rows // tile_side
    column_block = lax.all_gather(features, "row", axis=1, tiled=True)
    col_source = column_block.reshape(-1, tile_side, width)
    col_tiles = col_source.shape[0]
    partial_value = tile_aggregate(
        values, coords[1], coords[0], live_count, col_source, row_tiles, False, jnp.float32
    )
    partial_value = partial_value.reshape(n_col, sub_rows, width)
    share = scatter_sum(partial_value, "col")
    mixed = share.astype(jnp.bfloat16).reshape(sub_rows, width)
    pre = jnp.dot(mixed, weight_matrix, preferred_element_type=jnp.float32)
    sigma = jax.nn.sigmoid(pre)
    activated = (pre * sigma).astype(jnp.bfloat16)
    pre_grad = (
        out_grad.reshape(sub_rows, width).astype(jnp.float32) * sigma * (1.0 + pre * (1.0 - sigma))
    ).astype(jnp.bfloat16)
    weight_terms = jnp.dot(mixed.T, pre_grad, preferred_element_type=jnp.float32)
    own_grad = jnp.dot(pre_grad, weight_matrix.T, preferred_element_type=jnp.float32).astype(
        jnp.bfloat16
    )
    mixed_grad = lax.all_gather(own_grad.reshape(1, 1, sub_rows, width), "col", axis=1, tiled=True)
    weight_grad = all_sum(weight_terms)
    row_source = mixed_grad.reshape(row_tiles, tile_side, width)
    back_partial = tile_aggregate(
        values, coords[0], coords[1], live_count, row_source, col_tiles, True, jnp.bfloat16
    )
    back_partial = back_partial.reshape(n_row, sub_rows, width)
    feature_grad = row_reduce(back_partial, jnp.bfloat16).reshape(1, 1, sub_rows, width)
    return (activated.reshape(1, 1, sub_rows, width), feature_grad, weight_grad)


def solution(mesh):
    return jax.shard_map(
        shards,
        mesh=mesh,
        in_specs=(
            P("row", "col", None, None, None),
            P("row", "col", None, None),
            P("row", "col"),
            P("col", "row", None, None),
            P(),
            P("row", "col", None, None),
        ),
        out_specs=(P("row", "col", None, None), P("col", "row", None, None), P()),
        check_vma=False,
    )
```

```python
import jax
import jax.numpy as jnp
from jax import lax
from jax.experimental import pallas as pl
from jax.experimental.pallas import tpu as pltpu
from jax.sharding import PartitionSpec as P

GROUP = 32


def tile_aggregate(values, pick_index, place_index, live_count, source, segments, transposed, out_dtype):
    slot_total, tile_side, _ = values.shape
    width = source.shape[2]
    steps = slot_total // GROUP

    def kernel(picks_ref, places_ref, count_ref, vals_ref, src_ref, out_ref, acc_ref):
        step = pl.program_id(0)

        @pl.when(step == 0)
        def _():
            acc_ref[...] = jnp.zeros_like(acc_ref)

        def slot(j, carry):
            k = step * GROUP + j

            @pl.when(k < count_ref[0])
            def _():
                src_tile = src_ref[picks_ref[k]]
                tile = vals_ref[j]
                if transposed:
                    term = lax.dot_general(tile, src_tile, (((0,), (0,)), ((), ())),
                                           preferred_element_type=jnp.float32)
                else:
                    term = jnp.dot(tile, src_tile, preferred_element_type=jnp.float32)
                place = places_ref[k]
                acc_ref[place] += term

            return carry

        lax.fori_loop(0, GROUP, slot, 0)

        @pl.when(step == steps - 1)
        def _():
            out_ref[...] = acc_ref[...].astype(out_ref.dtype)

    def vals_map(i, picks, places, count):
        return (jnp.minimum(i, (count[0] - 1) // GROUP), 0, 0)

    grid_spec = pltpu.PrefetchScalarGridSpec(
        num_scalar_prefetch=3,
        grid=(steps,),
        in_specs=[
            pl.BlockSpec((GROUP, tile_side, tile_side), vals_map),
            pl.BlockSpec(source.shape, lambda i, *_: (0, 0, 0)),
        ],
        out_specs=pl.BlockSpec((segments, tile_side, width), lambda i, *_: (0, 0, 0)),
        scratch_shapes=[pltpu.VMEM((segments, tile_side, width), jnp.float32)],
    )
    flops = 2 * slot_total * tile_side * tile_side * width
    return pl.pallas_call(
        kernel,
        grid_spec=grid_spec,
        out_shape=jax.ShapeDtypeStruct((segments, tile_side, width), out_dtype),
        compiler_params=pltpu.CompilerParams(
            dimension_semantics=("arbitrary",), vmem_limit_bytes=48 * 1024 * 1024
        ),
        cost_estimate=pl.CostEstimate(
            flops=flops, transcendentals=0,
            bytes_accessed=values.size * 2 + source.size * 2 + segments * tile_side * width * jnp.dtype(out_dtype).itemsize,
        ),
    )(pick_index, place_index, live_count.reshape(1), values, source)


def scatter_sum(partial, axis_name):
    received = lax.all_to_all(partial, axis_name, 0, 0, tiled=True)
    return jnp.sum(received.astype(jnp.float32), axis=0)


def ring_step_pairs(size, stride, digits, shift):
    pairs = []
    for index in range(size):
        digit = (index // stride) % digits
        pairs.append((index, index + (((digit + shift) % digits) - digit) * stride))
    return pairs


def ring_reduce(partial, axis_name, stride, link_dtype):
    digits = partial.shape[0]
    size = lax.axis_size(axis_name)
    digit = (lax.axis_index(axis_name) // stride) % digits
    half = partial.shape[1] // 2
    lead = partial.shape[1]

    def block(offset):
        return lax.dynamic_index_in_dim(partial, (digit + offset) % digits, 0, keepdims=False)

    rightward = ring_step_pairs(size, stride, digits, 1)
    leftward = ring_step_pairs(size, stride, digits, -1)
    far = block(2)
    to_right = jnp.concatenate([block(1), far[:half]]).astype(link_dtype)
    to_left = jnp.concatenate([block(digits - 1), far[half:]]).astype(link_dtype)
    from_left = lax.ppermute(to_right, axis_name, rightward)
    from_right = lax.ppermute(to_left, axis_name, leftward)
    relay_left = lax.ppermute(from_left[lead:], axis_name, rightward)
    relay_right = lax.ppermute(from_right[lead:], axis_name, leftward)
    total = block(0).astype(jnp.float32) + from_left[:lead].astype(jnp.float32)
    total = total + from_right[:lead].astype(jnp.float32)
    return total + jnp.concatenate([relay_left, relay_right]).astype(jnp.float32)


def pair_reduce(partial, axis_name, stride, link_dtype):
    size = lax.axis_size(axis_name)
    digit = (lax.axis_index(axis_name) // stride) % 2
    pairs = [(index, index ^ stride) for index in range(size)]
    mine = lax.dynamic_index_in_dim(partial, digit, 0, keepdims=False)
    other = lax.dynamic_index_in_dim(partial, 1 - digit, 0, keepdims=False)
    return mine.astype(jnp.float32) + lax.ppermute(other.astype(link_dtype), axis_name, pairs).astype(jnp.float32)


def digit_of(axis_name, stride, digits):
    return (lax.axis_index(axis_name) // stride) % digits


def pair_gather(block, axis_name, stride):
    size = lax.axis_size(axis_name)
    other = lax.ppermute(block, axis_name, [(index, index ^ stride) for index in range(size)])
    first = digit_of(axis_name, stride, 2) == 0
    return jnp.stack([jnp.where(first, block, other), jnp.where(first, other, block)])


def ring_gather(block, axis_name, stride):
    size = lax.axis_size(axis_name)
    rightward = ring_step_pairs(size, stride, 4, 1)
    leftward = ring_step_pairs(size, stride, 4, -1)
    half = block.shape[0] // 2
    from_left = lax.ppermute(block, axis_name, rightward)
    from_right = lax.ppermute(block, axis_name, leftward)
    far_low = lax.ppermute(from_left[:half], axis_name, rightward)
    far_high = lax.ppermute(from_right[half:], axis_name, leftward)
    far = jnp.concatenate([far_low, far_high])
    by_offset = jnp.stack([block, from_right, far, from_left])
    return jnp.roll(by_offset, digit_of(axis_name, stride, 4), axis=0)


def line_gather(block, axis_name, stride):
    size = lax.axis_size(axis_name)
    parts = [block]
    for shift in (3, 2, 1):
        parts.append(lax.ppermute(block, axis_name, ring_step_pairs(size, stride, 4, shift)))
    return jnp.roll(jnp.stack(parts), digit_of(axis_name, stride, 4), axis=0)


def line_reduce(partial, axis_name, stride, link_dtype):
    size = lax.axis_size(axis_name)
    digit = digit_of(axis_name, stride, 4)
    total = lax.dynamic_index_in_dim(partial, digit, 0, keepdims=False).astype(jnp.float32)
    for shift in (1, 2, 3):
        outgoing = lax.dynamic_index_in_dim(partial, (digit + shift) % 4, 0, keepdims=False)
        incoming = lax.ppermute(outgoing.astype(link_dtype), axis_name, ring_step_pairs(size, stride, 4, shift))
        total = total + incoming.astype(jnp.float32)
    return total


def row_gather(block):
    pair = pair_gather(block, "row", 4)
    plane = jnp.swapaxes(ring_gather(pair, "row", 1), 0, 1)
    plane = plane.reshape((8,) + block.shape)
    return ring_gather(plane, "row", 8).reshape((32,) + block.shape)


def col_gather(block):
    pair = pair_gather(block, "col", 1)
    return line_gather(pair, "col", 2).reshape((8,) + block.shape)


def col_reduce(partial, link_dtype):
    core = digit_of("col", 1, 2)
    size = lax.axis_size("col")
    split = partial.reshape((4, 2) + partial.shape[1:])
    mine = lax.dynamic_index_in_dim(split, core, 1, keepdims=False).astype(jnp.float32)
    other = lax.dynamic_index_in_dim(split, 1 - core, 1, keepdims=False).astype(link_dtype)
    swapped = lax.ppermute(other, "col", [(index, index ^ 1) for index in range(size)])
    return line_reduce(mine + swapped.astype(jnp.float32), "col", 2, link_dtype)


def row_reduce(partial, link_dtype):
    count, rows, width = partial.shape
    split = width // 2
    first = partial[:, :, :split].reshape(4, 8, rows, split)
    first = ring_reduce(first, "row", 8, link_dtype).reshape(2, 4, rows, split)
    first = jnp.swapaxes(first, 0, 1)
    first = ring_reduce(first, "row", 1, link_dtype)
    second = partial[:, :, split:].reshape(4, 2, 4, rows, split)
    second = jnp.transpose(second, (2, 0, 1, 3, 4))
    second = ring_reduce(second, "row", 1, link_dtype).reshape(4, 2, rows, split)
    second = ring_reduce(second, "row", 8, link_dtype)
    both = jnp.concatenate([first, second], axis=-1)
    return pair_reduce(both, "row", 4, link_dtype)


def all_sum(terms):
    axes = ("row", "col")
    count = lax.axis_size("row") * lax.axis_size("col")
    rows, width = terms.shape
    pieces = terms.reshape(count, rows // count, width)
    mine = jnp.sum(lax.all_to_all(pieces, axes, 0, 0, tiled=True), axis=0, keepdims=True)
    spread = jnp.broadcast_to(mine, (count, rows // count, width))
    return lax.all_to_all(spread, axes, 0, 0, tiled=True).reshape(rows, width)


def shards(tile_values, tile_coords, tile_counts, features, weight_matrix, out_grad):
    values = tile_values[0, 0]
    coords = tile_coords[0, 0]
    live_count = tile_counts[0, 0]
    tile_side = values.shape[1]
    sub_rows = features.shape[2]
    width = features.shape[3]
    n_col = lax.axis_size("col")
    n_row = lax.axis_size("row")
    row_tiles = n_col * sub_rows // tile_side
    column_block = row_gather(features.reshape(sub_rows, width))
    col_source = column_block.reshape(-1, tile_side, width)
    col_tiles = col_source.shape[0]
    partial_value = tile_aggregate(
        values, coords[1], coords[0], live_count, col_source, row_tiles, False, jnp.float32
    )
    partial_value = partial_value.reshape(n_col, sub_rows, width)
    share = col_reduce(partial_value, jnp.float32)
    mixed = share.astype(jnp.bfloat16).reshape(sub_rows, width)
    pre = jnp.dot(mixed, weight_matrix, preferred_element_type=jnp.float32)
    sigma = jax.nn.sigmoid(pre)
    activated = (pre * sigma).astype(jnp.bfloat16)
    pre_grad = (
        out_grad.reshape(sub_rows, width).astype(jnp.float32) * sigma * (1.0 + pre * (1.0 - sigma))
    ).astype(jnp.bfloat16)
    weight_terms = jnp.dot(mixed.T, pre_grad, preferred_element_type=jnp.float32)
    own_grad = jnp.dot(pre_grad, weight_matrix.T, preferred_element_type=jnp.float32).astype(
        jnp.bfloat16
    )
    mixed_grad = col_gather(own_grad)
    weight_grad = all_sum(weight_terms)
    row_source = mixed_grad.reshape(row_tiles, tile_side, width)
    back_partial = tile_aggregate(
        values, coords[0], coords[1], live_count, row_source, col_tiles, True, jnp.bfloat16
    )
    back_partial = back_partial.reshape(n_row, sub_rows, width)
    feature_grad = row_reduce(back_partial, jnp.bfloat16).reshape(1, 1, sub_rows, width)
    return (activated.reshape(1, 1, sub_rows, width), feature_grad, weight_grad)


def solution(mesh):
    return jax.shard_map(
        shards,
        mesh=mesh,
        in_specs=(
            P("row", "col", None, None, None),
            P("row", "col", None, None),
            P("row", "col"),
            P("col", "row", None, None),
            P(),
            P("row", "col", None, None),
        ),
        out_specs=(P("row", "col", None, None), P("col", "row", None, None), P()),
        check_vma=False,
    )
```

```python
import jax
import jax.numpy as jnp
from jax import lax
from jax.experimental import pallas as pl
from jax.experimental.pallas import tpu as pltpu
from jax.sharding import PartitionSpec as P


def tile_aggregate(values, pick_index, place_index, live_count, source, segments, transposed, out_dtype):
    slot_total, tile_side, _ = values.shape
    width = source.shape[2]

    def kernel(picks_ref, places_ref, count_ref, vals_ref, src_ref, out_ref, acc_ref):
        acc_ref[...] = jnp.zeros_like(acc_ref)

        def slot(k, carry):
            src_tile = src_ref[picks_ref[k]]
            tile = vals_ref[k]
            if transposed:
                term = lax.dot_general(tile, src_tile, (((0,), (0,)), ((), ())),
                                       preferred_element_type=jnp.float32)
            else:
                term = jnp.dot(tile, src_tile, preferred_element_type=jnp.float32)
            acc_ref[places_ref[k]] += term
            return carry

        lax.fori_loop(0, count_ref[0], slot, 0)
        out_ref[...] = acc_ref[...].astype(out_ref.dtype)

    whole = lambda i, *_: (0, 0, 0)
    grid_spec = pltpu.PrefetchScalarGridSpec(
        num_scalar_prefetch=3,
        grid=(1,),
        in_specs=[
            pl.BlockSpec(values.shape, whole, pipeline_mode=pl.Buffered(1)),
            pl.BlockSpec(source.shape, whole, pipeline_mode=pl.Buffered(1)),
        ],
        out_specs=pl.BlockSpec((segments, tile_side, width), whole, pipeline_mode=pl.Buffered(1)),
        scratch_shapes=[pltpu.VMEM((segments, tile_side, width), jnp.float32)],
    )
    flops = 2 * slot_total * tile_side * tile_side * width
    return pl.pallas_call(
        kernel,
        grid_spec=grid_spec,
        out_shape=jax.ShapeDtypeStruct((segments, tile_side, width), out_dtype),
        compiler_params=pltpu.CompilerParams(vmem_limit_bytes=56 * 1024 * 1024),
        cost_estimate=pl.CostEstimate(
            flops=flops, transcendentals=0,
            bytes_accessed=values.size * 2 + source.size * 2 + segments * tile_side * width * jnp.dtype(out_dtype).itemsize,
        ),
    )(pick_index, place_index, live_count.reshape(1), values, source)


def scatter_sum(partial, axis_name):
    received = lax.all_to_all(partial, axis_name, 0, 0, tiled=True)
    return jnp.sum(received.astype(jnp.float32), axis=0)


def ring_step_pairs(size, stride, digits, shift):
    pairs = []
    for index in range(size):
        digit = (index // stride) % digits
        pairs.append((index, index + (((digit + shift) % digits) - digit) * stride))
    return pairs


def ring_reduce(partial, axis_name, stride, link_dtype):
    digits = partial.shape[0]
    size = lax.axis_size(axis_name)
    digit = (lax.axis_index(axis_name) // stride) % digits
    half = partial.shape[1] // 2
    lead = partial.shape[1]

    def block(offset):
        return lax.dynamic_index_in_dim(partial, (digit + offset) % digits, 0, keepdims=False)

    rightward = ring_step_pairs(size, stride, digits, 1)
    leftward = ring_step_pairs(size, stride, digits, -1)
    far = block(2)
    to_right = jnp.concatenate([block(1), far[:half]]).astype(link_dtype)
    to_left = jnp.concatenate([block(digits - 1), far[half:]]).astype(link_dtype)
    from_left = lax.ppermute(to_right, axis_name, rightward)
    from_right = lax.ppermute(to_left, axis_name, leftward)
    relay_left = lax.ppermute(from_left[lead:], axis_name, rightward)
    relay_right = lax.ppermute(from_right[lead:], axis_name, leftward)
    total = block(0).astype(jnp.float32) + from_left[:lead].astype(jnp.float32)
    total = total + from_right[:lead].astype(jnp.float32)
    return total + jnp.concatenate([relay_left, relay_right]).astype(jnp.float32)


def pair_reduce(partial, axis_name, stride, link_dtype):
    size = lax.axis_size(axis_name)
    digit = (lax.axis_index(axis_name) // stride) % 2
    pairs = [(index, index ^ stride) for index in range(size)]
    mine = lax.dynamic_index_in_dim(partial, digit, 0, keepdims=False)
    other = lax.dynamic_index_in_dim(partial, 1 - digit, 0, keepdims=False)
    return mine.astype(jnp.float32) + lax.ppermute(other.astype(link_dtype), axis_name, pairs).astype(jnp.float32)


def digit_of(axis_name, stride, digits):
    return (lax.axis_index(axis_name) // stride) % digits


def pair_gather(block, axis_name, stride):
    size = lax.axis_size(axis_name)
    other = lax.ppermute(block, axis_name, [(index, index ^ stride) for index in range(size)])
    first = digit_of(axis_name, stride, 2) == 0
    return jnp.stack([jnp.where(first, block, other), jnp.where(first, other, block)])


def ring_gather(block, axis_name, stride):
    size = lax.axis_size(axis_name)
    rightward = ring_step_pairs(size, stride, 4, 1)
    leftward = ring_step_pairs(size, stride, 4, -1)
    half = block.shape[0] // 2
    from_left = lax.ppermute(block, axis_name, rightward)
    from_right = lax.ppermute(block, axis_name, leftward)
    far_low = lax.ppermute(from_left[:half], axis_name, rightward)
    far_high = lax.ppermute(from_right[half:], axis_name, leftward)
    far = jnp.concatenate([far_low, far_high])
    by_offset = jnp.stack([block, from_right, far, from_left])
    return jnp.roll(by_offset, digit_of(axis_name, stride, 4), axis=0)


def line_gather(block, axis_name, stride):
    size = lax.axis_size(axis_name)
    parts = [block]
    for shift in (3, 2, 1):
        parts.append(lax.ppermute(block, axis_name, ring_step_pairs(size, stride, 4, shift)))
    return jnp.roll(jnp.stack(parts), digit_of(axis_name, stride, 4), axis=0)


def line_reduce(partial, axis_name, stride, link_dtype):
    size = lax.axis_size(axis_name)
    digit = digit_of(axis_name, stride, 4)
    total = lax.dynamic_index_in_dim(partial, digit, 0, keepdims=False).astype(jnp.float32)
    for shift in (1, 2, 3):
        outgoing = lax.dynamic_index_in_dim(partial, (digit + shift) % 4, 0, keepdims=False)
        incoming = lax.ppermute(outgoing.astype(link_dtype), axis_name, ring_step_pairs(size, stride, 4, shift))
        total = total + incoming.astype(jnp.float32)
    return total


def row_gather(block):
    pair = pair_gather(block, "row", 4)
    plane = jnp.swapaxes(ring_gather(pair, "row", 1), 0, 1)
    plane = plane.reshape((8,) + block.shape)
    return ring_gather(plane, "row", 8).reshape((32,) + block.shape)


def col_gather(block):
    pair = pair_gather(block, "col", 1)
    return line_gather(pair, "col", 2).reshape((8,) + block.shape)


def col_reduce(partial, link_dtype):
    core = digit_of("col", 1, 2)
    size = lax.axis_size("col")
    split = partial.reshape((4, 2) + partial.shape[1:])
    mine = lax.dynamic_index_in_dim(split, core, 1, keepdims=False).astype(jnp.float32)
    other = lax.dynamic_index_in_dim(split, 1 - core, 1, keepdims=False).astype(link_dtype)
    swapped = lax.ppermute(other, "col", [(index, index ^ 1) for index in range(size)])
    return line_reduce(mine + swapped.astype(jnp.float32), "col", 2, link_dtype)


def row_reduce(partial, link_dtype):
    count, rows, width = partial.shape
    split = width // 2
    first = partial[:, :, :split].reshape(4, 8, rows, split)
    first = ring_reduce(first, "row", 8, link_dtype).reshape(2, 4, rows, split)
    first = jnp.swapaxes(first, 0, 1)
    first = ring_reduce(first, "row", 1, link_dtype)
    second = partial[:, :, split:].reshape(4, 2, 4, rows, split)
    second = jnp.transpose(second, (2, 0, 1, 3, 4))
    second = ring_reduce(second, "row", 1, link_dtype).reshape(4, 2, rows, split)
    second = ring_reduce(second, "row", 8, link_dtype)
    both = jnp.concatenate([first, second], axis=-1)
    return pair_reduce(both, "row", 4, link_dtype)


def all_sum(terms):
    axes = ("row", "col")
    count = lax.axis_size("row") * lax.axis_size("col")
    rows, width = terms.shape
    pieces = terms.reshape(count, rows // count, width)
    mine = jnp.sum(lax.all_to_all(pieces, axes, 0, 0, tiled=True), axis=0, keepdims=True)
    spread = jnp.broadcast_to(mine, (count, rows // count, width))
    return lax.all_to_all(spread, axes, 0, 0, tiled=True).reshape(rows, width)


def shards(tile_values, tile_coords, tile_counts, features, weight_matrix, out_grad):
    values = tile_values[0, 0]
    coords = tile_coords[0, 0]
    live_count = tile_counts[0, 0]
    tile_side = values.shape[1]
    sub_rows = features.shape[2]
    width = features.shape[3]
    n_col = lax.axis_size("col")
    n_row = lax.axis_size("row")
    row_tiles = n_col * sub_rows // tile_side
    column_block = row_gather(features.reshape(sub_rows, width))
    col_source = column_block.reshape(-1, tile_side, width)
    col_tiles = col_source.shape[0]
    partial_value = tile_aggregate(
        values, coords[1], coords[0], live_count, col_source, row_tiles, False, jnp.float32
    )
    partial_value = partial_value.reshape(n_col, sub_rows, width)
    share = col_reduce(partial_value, jnp.float32)
    mixed = share.astype(jnp.bfloat16).reshape(sub_rows, width)
    pre = jnp.dot(mixed, weight_matrix, preferred_element_type=jnp.float32)
    sigma = jax.nn.sigmoid(pre)
    activated = (pre * sigma).astype(jnp.bfloat16)
    pre_grad = (
        out_grad.reshape(sub_rows, width).astype(jnp.float32) * sigma * (1.0 + pre * (1.0 - sigma))
    ).astype(jnp.bfloat16)
    weight_terms = jnp.dot(mixed.T, pre_grad, preferred_element_type=jnp.float32)
    own_grad = jnp.dot(pre_grad, weight_matrix.T, preferred_element_type=jnp.float32).astype(
        jnp.bfloat16
    )
    mixed_grad = col_gather(own_grad)
    weight_grad = all_sum(weight_terms)
    row_source = mixed_grad.reshape(row_tiles, tile_side, width)
    back_partial = tile_aggregate(
        values, coords[0], coords[1], live_count, row_source, col_tiles, True, jnp.bfloat16
    )
    back_partial = back_partial.reshape(n_row, sub_rows, width)
    feature_grad = row_reduce(back_partial, jnp.bfloat16).reshape(1, 1, sub_rows, width)
    return (activated.reshape(1, 1, sub_rows, width), feature_grad, weight_grad)


def solution(mesh):
    return jax.shard_map(
        shards,
        mesh=mesh,
        in_specs=(
            P("row", "col", None, None, None),
            P("row", "col", None, None),
            P("row", "col"),
            P("col", "row", None, None),
            P(),
            P("row", "col", None, None),
        ),
        out_specs=(P("row", "col", None, None), P("col", "row", None, None), P()),
        check_vma=False,
    )
```

```python
import jax
import jax.numpy as jnp
from jax import lax
from jax.experimental import pallas as pl
from jax.experimental.pallas import tpu as pltpu
from jax.sharding import PartitionSpec as P


def tile_aggregate(values, pick_index, place_index, live_count, source, segments, transposed, out_dtype):
    slot_total, tile_side, _ = values.shape
    width = source.shape[2]
    slot_ids = jnp.arange(slot_total, dtype=jnp.int32)
    place_index = jnp.where(slot_ids < live_count, place_index, segments)

    def kernel(picks_ref, places_ref, vals_ref, src_ref, out_ref, acc_ref):
        acc_ref[...] = jnp.zeros_like(acc_ref)

        def one(k):
            src_tile = src_ref[picks_ref[k]]
            tile = vals_ref[k]
            if transposed:
                term = lax.dot_general(tile, src_tile, (((0,), (0,)), ((), ())),
                                       preferred_element_type=jnp.float32)
            else:
                term = jnp.dot(tile, src_tile, preferred_element_type=jnp.float32)
            acc_ref[places_ref[k]] += term

        def pair(p, carry):
            one(2 * p)
            one(2 * p + 1)
            return carry

        lax.fori_loop(0, slot_total // 2, pair, 0)
        out_ref[...] = acc_ref[:segments].astype(out_ref.dtype)

    whole = lambda i, *_: (0, 0, 0)
    grid_spec = pltpu.PrefetchScalarGridSpec(
        num_scalar_prefetch=2,
        grid=(1,),
        in_specs=[
            pl.BlockSpec(values.shape, whole, pipeline_mode=pl.Buffered(1)),
            pl.BlockSpec(source.shape, whole, pipeline_mode=pl.Buffered(1)),
        ],
        out_specs=pl.BlockSpec((segments, tile_side, width), whole, pipeline_mode=pl.Buffered(1)),
        scratch_shapes=[pltpu.VMEM((segments + 1, tile_side, width), jnp.float32)],
    )
    flops = 2 * slot_total * tile_side * tile_side * width
    return pl.pallas_call(
        kernel,
        grid_spec=grid_spec,
        out_shape=jax.ShapeDtypeStruct((segments, tile_side, width), out_dtype),
        compiler_params=pltpu.CompilerParams(vmem_limit_bytes=56 * 1024 * 1024),
        cost_estimate=pl.CostEstimate(
            flops=flops, transcendentals=0,
            bytes_accessed=values.size * 2 + source.size * 2 + segments * tile_side * width * jnp.dtype(out_dtype).itemsize,
        ),
    )(pick_index, place_index, values, source)


def scatter_sum(partial, axis_name):
    received = lax.all_to_all(partial, axis_name, 0, 0, tiled=True)
    return jnp.sum(received.astype(jnp.float32), axis=0)


def ring_step_pairs(size, stride, digits, shift):
    pairs = []
    for index in range(size):
        digit = (index // stride) % digits
        pairs.append((index, index + (((digit + shift) % digits) - digit) * stride))
    return pairs


def ring_reduce(partial, axis_name, stride, link_dtype):
    digits = partial.shape[0]
    size = lax.axis_size(axis_name)
    digit = (lax.axis_index(axis_name) // stride) % digits
    half = partial.shape[1] // 2
    lead = partial.shape[1]

    def block(offset):
        return lax.dynamic_index_in_dim(partial, (digit + offset) % digits, 0, keepdims=False)

    rightward = ring_step_pairs(size, stride, digits, 1)
    leftward = ring_step_pairs(size, stride, digits, -1)
    far = block(2)
    to_right = jnp.concatenate([block(1), far[:half]]).astype(link_dtype)
    to_left = jnp.concatenate([block(digits - 1), far[half:]]).astype(link_dtype)
    from_left = lax.ppermute(to_right, axis_name, rightward)
    from_right = lax.ppermute(to_left, axis_name, leftward)
    relay_left = lax.ppermute(from_left[lead:], axis_name, rightward)
    relay_right = lax.ppermute(from_right[lead:], axis_name, leftward)
    total = block(0).astype(jnp.float32) + from_left[:lead].astype(jnp.float32)
    total = total + from_right[:lead].astype(jnp.float32)
    return total + jnp.concatenate([relay_left, relay_right]).astype(jnp.float32)


def pair_reduce(partial, axis_name, stride, link_dtype):
    size = lax.axis_size(axis_name)
    digit = (lax.axis_index(axis_name) // stride) % 2
    pairs = [(index, index ^ stride) for index in range(size)]
    mine = lax.dynamic_index_in_dim(partial, digit, 0, keepdims=False)
    other = lax.dynamic_index_in_dim(partial, 1 - digit, 0, keepdims=False)
    return mine.astype(jnp.float32) + lax.ppermute(other.astype(link_dtype), axis_name, pairs).astype(jnp.float32)


def digit_of(axis_name, stride, digits):
    return (lax.axis_index(axis_name) // stride) % digits


def pair_gather(block, axis_name, stride):
    size = lax.axis_size(axis_name)
    other = lax.ppermute(block, axis_name, [(index, index ^ stride) for index in range(size)])
    first = digit_of(axis_name, stride, 2) == 0
    return jnp.stack([jnp.where(first, block, other), jnp.where(first, other, block)])


def ring_gather(block, axis_name, stride):
    size = lax.axis_size(axis_name)
    rightward = ring_step_pairs(size, stride, 4, 1)
    leftward = ring_step_pairs(size, stride, 4, -1)
    half = block.shape[0] // 2
    from_left = lax.ppermute(block, axis_name, rightward)
    from_right = lax.ppermute(block, axis_name, leftward)
    far_low = lax.ppermute(from_left[:half], axis_name, rightward)
    far_high = lax.ppermute(from_right[half:], axis_name, leftward)
    far = jnp.concatenate([far_low, far_high])
    by_offset = jnp.stack([block, from_right, far, from_left])
    return jnp.roll(by_offset, digit_of(axis_name, stride, 4), axis=0)


def line_gather(block, axis_name, stride):
    size = lax.axis_size(axis_name)
    parts = [block]
    for shift in (3, 2, 1):
        parts.append(lax.ppermute(block, axis_name, ring_step_pairs(size, stride, 4, shift)))
    return jnp.roll(jnp.stack(parts), digit_of(axis_name, stride, 4), axis=0)


def line_reduce(partial, axis_name, stride, link_dtype):
    size = lax.axis_size(axis_name)
    digit = digit_of(axis_name, stride, 4)
    total = lax.dynamic_index_in_dim(partial, digit, 0, keepdims=False).astype(jnp.float32)
    for shift in (1, 2, 3):
        outgoing = lax.dynamic_index_in_dim(partial, (digit + shift) % 4, 0, keepdims=False)
        incoming = lax.ppermute(outgoing.astype(link_dtype), axis_name, ring_step_pairs(size, stride, 4, shift))
        total = total + incoming.astype(jnp.float32)
    return total


def row_gather(block):
    pair = pair_gather(block, "row", 4)
    plane = jnp.swapaxes(ring_gather(pair, "row", 1), 0, 1)
    plane = plane.reshape((8,) + block.shape)
    return ring_gather(plane, "row", 8).reshape((32,) + block.shape)


def col_gather(block):
    pair = pair_gather(block, "col", 1)
    return line_gather(pair, "col", 2).reshape((8,) + block.shape)


def col_reduce(partial, link_dtype):
    core = digit_of("col", 1, 2)
    size = lax.axis_size("col")
    split = partial.reshape((4, 2) + partial.shape[1:])
    mine = lax.dynamic_index_in_dim(split, core, 1, keepdims=False).astype(jnp.float32)
    other = lax.dynamic_index_in_dim(split, 1 - core, 1, keepdims=False).astype(link_dtype)
    swapped = lax.ppermute(other, "col", [(index, index ^ 1) for index in range(size)])
    return line_reduce(mine + swapped.astype(jnp.float32), "col", 2, link_dtype)


def row_reduce(partial, link_dtype):
    count, rows, width = partial.shape
    split = width // 2
    first = partial[:, :, :split].reshape(4, 8, rows, split)
    first = ring_reduce(first, "row", 8, link_dtype).reshape(2, 4, rows, split)
    first = jnp.swapaxes(first, 0, 1)
    first = ring_reduce(first, "row", 1, link_dtype)
    second = partial[:, :, split:].reshape(4, 2, 4, rows, split)
    second = jnp.transpose(second, (2, 0, 1, 3, 4))
    second = ring_reduce(second, "row", 1, link_dtype).reshape(4, 2, rows, split)
    second = ring_reduce(second, "row", 8, link_dtype)
    both = jnp.concatenate([first, second], axis=-1)
    return pair_reduce(both, "row", 4, link_dtype)


def all_sum(terms):
    axes = ("row", "col")
    count = lax.axis_size("row") * lax.axis_size("col")
    rows, width = terms.shape
    pieces = terms.reshape(count, rows // count, width)
    mine = jnp.sum(lax.all_to_all(pieces, axes, 0, 0, tiled=True), axis=0, keepdims=True)
    spread = jnp.broadcast_to(mine, (count, rows // count, width))
    return lax.all_to_all(spread, axes, 0, 0, tiled=True).reshape(rows, width)


def shards(tile_values, tile_coords, tile_counts, features, weight_matrix, out_grad):
    values = tile_values[0, 0]
    coords = tile_coords[0, 0]
    live_count = tile_counts[0, 0]
    tile_side = values.shape[1]
    sub_rows = features.shape[2]
    width = features.shape[3]
    n_col = lax.axis_size("col")
    n_row = lax.axis_size("row")
    row_tiles = n_col * sub_rows // tile_side
    column_block = row_gather(features.reshape(sub_rows, width))
    col_source = column_block.reshape(-1, tile_side, width)
    col_tiles = col_source.shape[0]
    partial_value = tile_aggregate(
        values, coords[1], coords[0], live_count, col_source, row_tiles, False, jnp.float32
    )
    partial_value = partial_value.reshape(n_col, sub_rows, width)
    share = col_reduce(partial_value, jnp.float32)
    mixed = share.astype(jnp.bfloat16).reshape(sub_rows, width)
    pre = jnp.dot(mixed, weight_matrix, preferred_element_type=jnp.float32)
    sigma = jax.nn.sigmoid(pre)
    activated = (pre * sigma).astype(jnp.bfloat16)
    pre_grad = (
        out_grad.reshape(sub_rows, width).astype(jnp.float32) * sigma * (1.0 + pre * (1.0 - sigma))
    ).astype(jnp.bfloat16)
    weight_terms = jnp.dot(mixed.T, pre_grad, preferred_element_type=jnp.float32)
    own_grad = jnp.dot(pre_grad, weight_matrix.T, preferred_element_type=jnp.float32).astype(
        jnp.bfloat16
    )
    mixed_grad = col_gather(own_grad)
    weight_grad = all_sum(weight_terms)
    row_source = mixed_grad.reshape(row_tiles, tile_side, width)
    back_partial = tile_aggregate(
        values, coords[0], coords[1], live_count, row_source, col_tiles, True, jnp.bfloat16
    )
    back_partial = back_partial.reshape(n_row, sub_rows, width)
    feature_grad = row_reduce(back_partial, jnp.bfloat16).reshape(1, 1, sub_rows, width)
    return (activated.reshape(1, 1, sub_rows, width), feature_grad, weight_grad)


def solution(mesh):
    return jax.shard_map(
        shards,
        mesh=mesh,
        in_specs=(
            P("row", "col", None, None, None),
            P("row", "col", None, None),
            P("row", "col"),
            P("col", "row", None, None),
            P(),
            P("row", "col", None, None),
        ),
        out_specs=(P("row", "col", None, None), P("col", "row", None, None), P()),
        check_vma=False,
    )
```

```python
import jax
import jax.numpy as jnp
from jax import lax
from jax.experimental import pallas as pl
from jax.experimental.pallas import tpu as pltpu
from jax.sharding import PartitionSpec as P


def tile_aggregate(values, pick_index, place_index, live_count, source, segments, transposed, out_dtype):
    slot_total, tile_side, _ = values.shape
    width = source.shape[2]
    slot_ids = jnp.arange(slot_total, dtype=jnp.int32)
    place_index = jnp.where(slot_ids < live_count, place_index, segments)

    def kernel(picks_ref, places_ref, vals_ref, src_ref, out_ref, acc_ref):
        acc_ref[...] = jnp.zeros_like(acc_ref)

        def one(k):
            src_tile = src_ref[picks_ref[k]]
            tile = vals_ref[k]
            if transposed:
                term = lax.dot_general(tile, src_tile, (((0,), (0,)), ((), ())),
                                       preferred_element_type=jnp.float32)
            else:
                term = jnp.dot(tile, src_tile, preferred_element_type=jnp.float32)
            acc_ref[places_ref[k]] += term

        def pair(p, carry):
            one(2 * p)
            one(2 * p + 1)
            return carry

        lax.fori_loop(0, slot_total // 2, pair, 0)
        out_ref[...] = acc_ref[:segments].astype(out_ref.dtype)

    whole = lambda i, *_: (0, 0, 0)
    grid_spec = pltpu.PrefetchScalarGridSpec(
        num_scalar_prefetch=2,
        grid=(1,),
        in_specs=[
            pl.BlockSpec(values.shape, whole, pipeline_mode=pl.Buffered(1)),
            pl.BlockSpec(source.shape, whole, pipeline_mode=pl.Buffered(1)),
        ],
        out_specs=pl.BlockSpec((segments, tile_side, width), whole, pipeline_mode=pl.Buffered(1)),
        scratch_shapes=[pltpu.VMEM((segments + 1, tile_side, width), jnp.float32)],
    )
    flops = 2 * slot_total * tile_side * tile_side * width
    return pl.pallas_call(
        kernel,
        grid_spec=grid_spec,
        out_shape=jax.ShapeDtypeStruct((segments, tile_side, width), out_dtype),
        compiler_params=pltpu.CompilerParams(vmem_limit_bytes=56 * 1024 * 1024),
        cost_estimate=pl.CostEstimate(
            flops=flops, transcendentals=0,
            bytes_accessed=values.size * 2 + source.size * 2 + segments * tile_side * width * jnp.dtype(out_dtype).itemsize,
        ),
    )(pick_index, place_index, values, source)


def scatter_sum(partial, axis_name):
    received = lax.all_to_all(partial, axis_name, 0, 0, tiled=True)
    return jnp.sum(received.astype(jnp.float32), axis=0)


def ring_step_pairs(size, stride, digits, shift):
    pairs = []
    for index in range(size):
        digit = (index // stride) % digits
        pairs.append((index, index + (((digit + shift) % digits) - digit) * stride))
    return pairs


def ring_reduce(partial, axis_name, stride, link_dtype):
    digits = partial.shape[0]
    size = lax.axis_size(axis_name)
    digit = (lax.axis_index(axis_name) // stride) % digits
    half = partial.shape[1] // 2
    lead = partial.shape[1]

    def block(offset):
        return lax.dynamic_index_in_dim(partial, (digit + offset) % digits, 0, keepdims=False)

    rightward = ring_step_pairs(size, stride, digits, 1)
    leftward = ring_step_pairs(size, stride, digits, -1)
    far = block(2)
    to_right = jnp.concatenate([block(1), far[:half]]).astype(link_dtype)
    to_left = jnp.concatenate([block(digits - 1), far[half:]]).astype(link_dtype)
    from_left = lax.ppermute(to_right, axis_name, rightward)
    from_right = lax.ppermute(to_left, axis_name, leftward)
    relay_left = lax.ppermute(from_left[lead:], axis_name, rightward)
    relay_right = lax.ppermute(from_right[lead:], axis_name, leftward)
    total = block(0).astype(jnp.float32) + from_left[:lead].astype(jnp.float32)
    total = total + from_right[:lead].astype(jnp.float32)
    return total + jnp.concatenate([relay_left, relay_right]).astype(jnp.float32)


def pair_reduce(partial, axis_name, stride, link_dtype):
    size = lax.axis_size(axis_name)
    digit = (lax.axis_index(axis_name) // stride) % 2
    pairs = [(index, index ^ stride) for index in range(size)]
    mine = lax.dynamic_index_in_dim(partial, digit, 0, keepdims=False)
    other = lax.dynamic_index_in_dim(partial, 1 - digit, 0, keepdims=False)
    return mine.astype(jnp.float32) + lax.ppermute(other.astype(link_dtype), axis_name, pairs).astype(jnp.float32)


def digit_of(axis_name, stride, digits):
    return (lax.axis_index(axis_name) // stride) % digits


def pair_gather(block, axis_name, stride):
    size = lax.axis_size(axis_name)
    other = lax.ppermute(block, axis_name, [(index, index ^ stride) for index in range(size)])
    first = digit_of(axis_name, stride, 2) == 0
    return jnp.stack([jnp.where(first, block, other), jnp.where(first, other, block)])


def ring_gather(block, axis_name, stride):
    size = lax.axis_size(axis_name)
    rightward = ring_step_pairs(size, stride, 4, 1)
    leftward = ring_step_pairs(size, stride, 4, -1)
    half = block.shape[0] // 2
    from_left = lax.ppermute(block, axis_name, rightward)
    from_right = lax.ppermute(block, axis_name, leftward)
    far_low = lax.ppermute(from_left[:half], axis_name, rightward)
    far_high = lax.ppermute(from_right[half:], axis_name, leftward)
    far = jnp.concatenate([far_low, far_high])
    by_offset = jnp.stack([block, from_right, far, from_left])
    return jnp.roll(by_offset, digit_of(axis_name, stride, 4), axis=0)


def line_gather(block, axis_name, stride):
    size = lax.axis_size(axis_name)
    parts = [block]
    for shift in (3, 2, 1):
        parts.append(lax.ppermute(block, axis_name, ring_step_pairs(size, stride, 4, shift)))
    return jnp.roll(jnp.stack(parts), digit_of(axis_name, stride, 4), axis=0)


def line_reduce(partial, axis_name, stride, link_dtype):
    size = lax.axis_size(axis_name)
    digit = digit_of(axis_name, stride, 4)
    total = lax.dynamic_index_in_dim(partial, digit, 0, keepdims=False).astype(jnp.float32)
    for shift in (1, 2, 3):
        outgoing = lax.dynamic_index_in_dim(partial, (digit + shift) % 4, 0, keepdims=False)
        incoming = lax.ppermute(outgoing.astype(link_dtype), axis_name, ring_step_pairs(size, stride, 4, shift))
        total = total + incoming.astype(jnp.float32)
    return total


def row_gather(block):
    rows, width = block.shape
    split = width // 2
    pair = pair_gather(block, "row", 4)
    first = jnp.swapaxes(ring_gather(pair[..., :split], "row", 1), 0, 1)
    first = ring_gather(first.reshape(8, rows, split), "row", 8).reshape(32, rows, split)
    second = ring_gather(ring_gather(pair[..., split:], "row", 8), "row", 1)
    second = jnp.transpose(second, (1, 2, 0, 3, 4)).reshape(32, rows, split)
    return jnp.concatenate([first, second], axis=-1)


def col_gather(block):
    pair = pair_gather(block, "col", 1)
    return line_gather(pair, "col", 2).reshape((8,) + block.shape)


def col_reduce(partial, link_dtype):
    core = digit_of("col", 1, 2)
    size = lax.axis_size("col")
    split = partial.reshape((4, 2) + partial.shape[1:])
    mine = lax.dynamic_index_in_dim(split, core, 1, keepdims=False).astype(jnp.float32)
    other = lax.dynamic_index_in_dim(split, 1 - core, 1, keepdims=False).astype(link_dtype)
    swapped = lax.ppermute(other, "col", [(index, index ^ 1) for index in range(size)])
    return line_reduce(mine + swapped.astype(jnp.float32), "col", 2, link_dtype)


def row_reduce(partial, link_dtype):
    count, rows, width = partial.shape
    split = width // 2
    first = partial[:, :, :split].reshape(4, 8, rows, split)
    first = ring_reduce(first, "row", 8, link_dtype).reshape(2, 4, rows, split)
    first = jnp.swapaxes(first, 0, 1)
    first = ring_reduce(first, "row", 1, link_dtype)
    second = partial[:, :, split:].reshape(4, 2, 4, rows, split)
    second = jnp.transpose(second, (2, 0, 1, 3, 4))
    second = ring_reduce(second, "row", 1, link_dtype).reshape(4, 2, rows, split)
    second = ring_reduce(second, "row", 8, link_dtype)
    both = jnp.concatenate([first, second], axis=-1)
    return pair_reduce(both, "row", 4, link_dtype)


def all_sum(terms):
    axes = ("row", "col")
    count = lax.axis_size("row") * lax.axis_size("col")
    rows, width = terms.shape
    pieces = terms.reshape(count, rows // count, width)
    mine = jnp.sum(lax.all_to_all(pieces, axes, 0, 0, tiled=True), axis=0, keepdims=True)
    spread = jnp.broadcast_to(mine, (count, rows // count, width))
    return lax.all_to_all(spread, axes, 0, 0, tiled=True).reshape(rows, width)


def shards(tile_values, tile_coords, tile_counts, features, weight_matrix, out_grad):
    values = tile_values[0, 0]
    coords = tile_coords[0, 0]
    live_count = tile_counts[0, 0]
    tile_side = values.shape[1]
    sub_rows = features.shape[2]
    width = features.shape[3]
    n_col = lax.axis_size("col")
    n_row = lax.axis_size("row")
    row_tiles = n_col * sub_rows // tile_side
    column_block = row_gather(features.reshape(sub_rows, width))
    col_source = column_block.reshape(-1, tile_side, width)
    col_tiles = col_source.shape[0]
    partial_value = tile_aggregate(
        values, coords[1], coords[0], live_count, col_source, row_tiles, False, jnp.float32
    )
    partial_value = partial_value.reshape(n_col, sub_rows, width)
    share = col_reduce(partial_value, jnp.bfloat16)
    mixed = share.astype(jnp.bfloat16).reshape(sub_rows, width)
    pre = jnp.dot(mixed, weight_matrix, preferred_element_type=jnp.float32)
    sigma = jax.nn.sigmoid(pre)
    activated = (pre * sigma).astype(jnp.bfloat16)
    pre_grad = (
        out_grad.reshape(sub_rows, width).astype(jnp.float32) * sigma * (1.0 + pre * (1.0 - sigma))
    ).astype(jnp.bfloat16)
    weight_terms = jnp.dot(mixed.T, pre_grad, preferred_element_type=jnp.float32)
    own_grad = jnp.dot(pre_grad, weight_matrix.T, preferred_element_type=jnp.float32).astype(
        jnp.bfloat16
    )
    mixed_grad = col_gather(own_grad)
    weight_grad = all_sum(weight_terms)
    row_source = mixed_grad.reshape(row_tiles, tile_side, width)
    back_partial = tile_aggregate(
        values, coords[0], coords[1], live_count, row_source, col_tiles, True, jnp.bfloat16
    )
    back_partial = back_partial.reshape(n_row, sub_rows, width)
    feature_grad = row_reduce(back_partial, jnp.bfloat16).reshape(1, 1, sub_rows, width)
    return (activated.reshape(1, 1, sub_rows, width), feature_grad, weight_grad)


def solution(mesh):
    return jax.shard_map(
        shards,
        mesh=mesh,
        in_specs=(
            P("row", "col", None, None, None),
            P("row", "col", None, None),
            P("row", "col"),
            P("col", "row", None, None),
            P(),
            P("row", "col", None, None),
        ),
        out_specs=(P("row", "col", None, None), P("col", "row", None, None), P()),
        check_vma=False,
    )
```

```python
import jax
import jax.numpy as jnp
from jax import lax
from jax.experimental import pallas as pl
from jax.experimental.pallas import tpu as pltpu
from jax.sharding import PartitionSpec as P


def tile_aggregate(values, pick_index, place_index, live_count, source, segments, transposed, out_dtype):
    slot_total, tile_side, _ = values.shape
    width = source.shape[2]
    slot_ids = jnp.arange(slot_total, dtype=jnp.int32)
    place_index = jnp.where(slot_ids < live_count, place_index, segments)

    def kernel(picks_ref, places_ref, vals_ref, src_ref, out_ref, acc_ref):
        acc_ref[...] = jnp.zeros_like(acc_ref)

        def one(k):
            src_tile = src_ref[picks_ref[k]]
            tile = vals_ref[k]
            if transposed:
                term = lax.dot_general(tile, src_tile, (((0,), (0,)), ((), ())),
                                       preferred_element_type=jnp.float32)
            else:
                term = jnp.dot(tile, src_tile, preferred_element_type=jnp.float32)
            acc_ref[places_ref[k]] += term

        def pair(p, carry):
            one(2 * p)
            one(2 * p + 1)
            return carry

        lax.fori_loop(0, slot_total // 2, pair, 0)
        out_ref[...] = acc_ref[:segments].astype(out_ref.dtype)

    whole = lambda i, *_: (0, 0, 0)
    grid_spec = pltpu.PrefetchScalarGridSpec(
        num_scalar_prefetch=2,
        grid=(1,),
        in_specs=[
            pl.BlockSpec(values.shape, whole, pipeline_mode=pl.Buffered(1)),
            pl.BlockSpec(source.shape, whole, pipeline_mode=pl.Buffered(1)),
        ],
        out_specs=pl.BlockSpec((segments, tile_side, width), whole, pipeline_mode=pl.Buffered(1)),
        scratch_shapes=[pltpu.VMEM((segments + 1, tile_side, width), jnp.float32)],
    )
    flops = 2 * slot_total * tile_side * tile_side * width
    return pl.pallas_call(
        kernel,
        grid_spec=grid_spec,
        out_shape=jax.ShapeDtypeStruct((segments, tile_side, width), out_dtype),
        compiler_params=pltpu.CompilerParams(vmem_limit_bytes=56 * 1024 * 1024),
        cost_estimate=pl.CostEstimate(
            flops=flops, transcendentals=0,
            bytes_accessed=values.size * 2 + source.size * 2 + segments * tile_side * width * jnp.dtype(out_dtype).itemsize,
        ),
    )(pick_index, place_index, values, source)


def ring_step_pairs(size, stride, digits, shift):
    pairs = []
    for index in range(size):
        digit = (index // stride) % digits
        pairs.append((index, index + (((digit + shift) % digits) - digit) * stride))
    return pairs


def ring_reduce(partial, axis_name, stride, link_dtype):
    digits = partial.shape[0]
    size = lax.axis_size(axis_name)
    digit = (lax.axis_index(axis_name) // stride) % digits
    half = partial.shape[1] // 2
    lead = partial.shape[1]

    def block(offset):
        return lax.dynamic_index_in_dim(partial, (digit + offset) % digits, 0, keepdims=False)

    rightward = ring_step_pairs(size, stride, digits, 1)
    leftward = ring_step_pairs(size, stride, digits, -1)
    far = block(2)
    to_right = jnp.concatenate([block(1), far[:half]]).astype(link_dtype)
    to_left = jnp.concatenate([block(digits - 1), far[half:]]).astype(link_dtype)
    from_left = lax.ppermute(to_right, axis_name, rightward)
    from_right = lax.ppermute(to_left, axis_name, leftward)
    relay_left = lax.ppermute(from_left[lead:], axis_name, rightward)
    relay_right = lax.ppermute(from_right[lead:], axis_name, leftward)
    total = block(0).astype(jnp.float32) + from_left[:lead].astype(jnp.float32)
    total = total + from_right[:lead].astype(jnp.float32)
    return total + jnp.concatenate([relay_left, relay_right]).astype(jnp.float32)


def pair_reduce(partial, axis_name, stride, link_dtype):
    size = lax.axis_size(axis_name)
    digit = (lax.axis_index(axis_name) // stride) % 2
    pairs = [(index, index ^ stride) for index in range(size)]
    mine = lax.dynamic_index_in_dim(partial, digit, 0, keepdims=False)
    other = lax.dynamic_index_in_dim(partial, 1 - digit, 0, keepdims=False)
    return mine.astype(jnp.float32) + lax.ppermute(other.astype(link_dtype), axis_name, pairs).astype(jnp.float32)


def digit_of(axis_name, stride, digits):
    return (lax.axis_index(axis_name) // stride) % digits


def pair_gather(block, axis_name, stride):
    size = lax.axis_size(axis_name)
    other = lax.ppermute(block, axis_name, [(index, index ^ stride) for index in range(size)])
    first = digit_of(axis_name, stride, 2) == 0
    return jnp.stack([jnp.where(first, block, other), jnp.where(first, other, block)])


def ring_gather(block, axis_name, stride):
    size = lax.axis_size(axis_name)
    rightward = ring_step_pairs(size, stride, 4, 1)
    leftward = ring_step_pairs(size, stride, 4, -1)
    half = block.shape[0] // 2
    from_left = lax.ppermute(block, axis_name, rightward)
    from_right = lax.ppermute(block, axis_name, leftward)
    far_low = lax.ppermute(from_left[:half], axis_name, rightward)
    far_high = lax.ppermute(from_right[half:], axis_name, leftward)
    far = jnp.concatenate([far_low, far_high])
    by_offset = jnp.stack([block, from_right, far, from_left])
    return jnp.roll(by_offset, digit_of(axis_name, stride, 4), axis=0)


def line_gather(block, axis_name, stride):
    size = lax.axis_size(axis_name)
    parts = [block]
    for shift in (3, 2, 1):
        parts.append(lax.ppermute(block, axis_name, ring_step_pairs(size, stride, 4, shift)))
    return jnp.roll(jnp.stack(parts), digit_of(axis_name, stride, 4), axis=0)


def line_reduce(partial, axis_name, stride, link_dtype):
    size = lax.axis_size(axis_name)
    digit = digit_of(axis_name, stride, 4)
    total = lax.dynamic_index_in_dim(partial, digit, 0, keepdims=False).astype(jnp.float32)
    for shift in (1, 2, 3):
        outgoing = lax.dynamic_index_in_dim(partial, (digit + shift) % 4, 0, keepdims=False)
        incoming = lax.ppermute(outgoing.astype(link_dtype), axis_name, ring_step_pairs(size, stride, 4, shift))
        total = total + incoming.astype(jnp.float32)
    return total


def row_gather(block):
    rows, width = block.shape
    split = width // 2
    pair = pair_gather(block, "row", 4)
    first = jnp.swapaxes(ring_gather(pair[..., :split], "row", 1), 0, 1)
    first = ring_gather(first.reshape(8, rows, split), "row", 8).reshape(32, rows, split)
    second = ring_gather(ring_gather(pair[..., split:], "row", 8), "row", 1)
    second = jnp.transpose(second, (1, 2, 0, 3, 4)).reshape(32, rows, split)
    return jnp.concatenate([first, second], axis=-1)


def col_gather(block):
    pair = pair_gather(block, "col", 1)
    return line_gather(pair, "col", 2).reshape((8,) + block.shape)


def col_reduce(partial, link_dtype):
    core = digit_of("col", 1, 2)
    size = lax.axis_size("col")
    split = partial.reshape((4, 2) + partial.shape[1:])
    mine = lax.dynamic_index_in_dim(split, core, 1, keepdims=False).astype(jnp.float32)
    other = lax.dynamic_index_in_dim(split, 1 - core, 1, keepdims=False).astype(link_dtype)
    swapped = lax.ppermute(other, "col", [(index, index ^ 1) for index in range(size)])
    return line_reduce(mine + swapped.astype(jnp.float32), "col", 2, link_dtype)


def row_reduce(partial, link_dtype):
    _, rows, width = partial.shape
    split = width // 2
    first = partial[:, :, :split].reshape(4, 8, rows, split)
    first = ring_reduce(first, "row", 8, link_dtype).reshape(2, 4, rows, split)
    first = jnp.swapaxes(first, 0, 1)
    first = ring_reduce(first, "row", 1, link_dtype)
    second = partial[:, :, split:].reshape(4, 2, 4, rows, split)
    second = jnp.transpose(second, (2, 0, 1, 3, 4))
    second = ring_reduce(second, "row", 1, link_dtype).reshape(4, 2, rows, split)
    second = ring_reduce(second, "row", 8, link_dtype)
    both = jnp.concatenate([first, second], axis=-1)
    return pair_reduce(both, "row", 4, link_dtype)


def all_sum(terms):
    axes = ("row", "col")
    count = lax.axis_size("row") * lax.axis_size("col")
    rows, width = terms.shape
    pieces = terms.reshape(count, rows // count, width)
    spread_in = lax.all_to_all(pieces, axes, 0, 0, tiled=True)
    mine = jnp.sum(spread_in, axis=0, keepdims=True)
    spread = jnp.broadcast_to(mine, (count, rows // count, width))
    return lax.all_to_all(spread, axes, 0, 0, tiled=True).reshape(rows, width)


def layer(tile_values, tile_coords, tile_counts, features, weight_matrix, out_grad):
    values = tile_values[0, 0]
    coords = tile_coords[0, 0]
    live_count = tile_counts[0, 0]
    tile_side = values.shape[1]
    sub_rows = features.shape[2]
    width = features.shape[3]
    n_col = lax.axis_size("col")
    n_row = lax.axis_size("row")
    row_tiles = n_col * sub_rows // tile_side
    column_block = row_gather(features.reshape(sub_rows, width))
    col_source = column_block.reshape(-1, tile_side, width)
    col_tiles = col_source.shape[0]
    partial_value = tile_aggregate(
        values, coords[1], coords[0], live_count, col_source, row_tiles, False, jnp.float32
    )
    partial_value = partial_value.reshape(n_col, sub_rows, width)
    share = col_reduce(partial_value, jnp.bfloat16)
    mixed = share.astype(jnp.bfloat16).reshape(sub_rows, width)
    pre = jnp.dot(mixed, weight_matrix, preferred_element_type=jnp.float32)
    sigma = jax.nn.sigmoid(pre)
    activated = (pre * sigma).astype(jnp.bfloat16)
    pre_grad = (
        out_grad.reshape(sub_rows, width).astype(jnp.float32) * sigma * (1.0 + pre * (1.0 - sigma))
    ).astype(jnp.bfloat16)
    weight_terms = jnp.dot(mixed.T, pre_grad, preferred_element_type=jnp.float32)
    own_grad = jnp.dot(pre_grad, weight_matrix.T, preferred_element_type=jnp.float32).astype(
        jnp.bfloat16
    )
    mixed_grad = col_gather(own_grad)
    weight_grad = all_sum(weight_terms)
    row_source = mixed_grad.reshape(row_tiles, tile_side, width)
    back_partial = tile_aggregate(values, coords[0], coords[1], live_count, row_source, col_tiles, True, jnp.bfloat16)
    back_partial = back_partial.reshape(n_row, sub_rows, width)
    feature_grad = row_reduce(back_partial, jnp.bfloat16).reshape(1, 1, sub_rows, width)
    return (activated.reshape(1, 1, sub_rows, width), feature_grad, weight_grad)


def solution(mesh):
    return jax.shard_map(
        layer,
        mesh=mesh,
        in_specs=(
            P("row", "col", None, None, None),
            P("row", "col", None, None),
            P("row", "col"),
            P("col", "row", None, None),
            P(),
            P("row", "col", None, None),
        ),
        out_specs=(P("row", "col", None, None), P("col", "row", None, None), P()),
        check_vma=False,
    )
```

```python
import jax
import jax.numpy as jnp
from jax import lax
from jax.experimental import pallas as pl
from jax.experimental.pallas import tpu as pltpu
from jax.sharding import PartitionSpec as P


def tile_aggregate(values, pick_index, place_index, live_count, source, segments, transposed, out_dtype):
    slot_total, tile_side, _ = values.shape
    width = source.shape[2]
    slot_ids = jnp.arange(slot_total, dtype=jnp.int32)
    place_index = jnp.where(slot_ids < live_count, place_index, segments)

    def kernel(picks_ref, places_ref, vals_ref, src_ref, out_ref, acc_ref):
        acc_ref[...] = jnp.zeros_like(acc_ref)

        def one(k):
            src_tile = src_ref[picks_ref[k]]
            tile = vals_ref[k]
            if transposed:
                term = lax.dot_general(tile, src_tile, (((0,), (0,)), ((), ())),
                                       preferred_element_type=jnp.float32)
            else:
                term = jnp.dot(tile, src_tile, preferred_element_type=jnp.float32)
            acc_ref[places_ref[k]] += term

        def pair(p, carry):
            one(2 * p)
            one(2 * p + 1)
            return carry

        lax.fori_loop(0, slot_total // 2, pair, 0)
        out_ref[...] = acc_ref[:segments].astype(out_ref.dtype)

    whole = lambda i, *_: (0, 0, 0)
    grid_spec = pltpu.PrefetchScalarGridSpec(
        num_scalar_prefetch=2,
        grid=(1,),
        in_specs=[
            pl.BlockSpec(values.shape, whole, pipeline_mode=pl.Buffered(1)),
            pl.BlockSpec(source.shape, whole, pipeline_mode=pl.Buffered(1)),
        ],
        out_specs=pl.BlockSpec((segments, tile_side, width), whole, pipeline_mode=pl.Buffered(1)),
        scratch_shapes=[pltpu.VMEM((segments + 1, tile_side, width), jnp.float32)],
    )
    flops = 2 * slot_total * tile_side * tile_side * width
    return pl.pallas_call(
        kernel,
        grid_spec=grid_spec,
        out_shape=jax.ShapeDtypeStruct((segments, tile_side, width), out_dtype),
        compiler_params=pltpu.CompilerParams(vmem_limit_bytes=56 * 1024 * 1024),
        cost_estimate=pl.CostEstimate(
            flops=flops, transcendentals=0,
            bytes_accessed=values.size * 2 + source.size * 2 + segments * tile_side * width * jnp.dtype(out_dtype).itemsize,
        ),
    )(pick_index, place_index, values, source)


def ring_step_pairs(size, stride, digits, shift):
    pairs = []
    for index in range(size):
        digit = (index // stride) % digits
        pairs.append((index, index + (((digit + shift) % digits) - digit) * stride))
    return pairs


def ring_reduce(partial, axis_name, stride, link_dtype):
    digits = partial.shape[0]
    size = lax.axis_size(axis_name)
    digit = (lax.axis_index(axis_name) // stride) % digits
    half = partial.shape[1] // 2
    lead = partial.shape[1]

    def block(offset):
        return lax.dynamic_index_in_dim(partial, (digit + offset) % digits, 0, keepdims=False)

    rightward = ring_step_pairs(size, stride, digits, 1)
    leftward = ring_step_pairs(size, stride, digits, -1)
    far = block(2)
    to_right = jnp.concatenate([block(1), far[:half]]).astype(link_dtype)
    to_left = jnp.concatenate([block(digits - 1), far[half:]]).astype(link_dtype)
    from_left = lax.ppermute(to_right, axis_name, rightward)
    from_right = lax.ppermute(to_left, axis_name, leftward)
    relay_left = lax.ppermute(from_left[lead:], axis_name, rightward)
    relay_right = lax.ppermute(from_right[lead:], axis_name, leftward)
    total = block(0).astype(jnp.float32) + from_left[:lead].astype(jnp.float32)
    total = total + from_right[:lead].astype(jnp.float32)
    return total + jnp.concatenate([relay_left, relay_right]).astype(jnp.float32)


def pair_reduce(partial, axis_name, stride, link_dtype):
    size = lax.axis_size(axis_name)
    digit = (lax.axis_index(axis_name) // stride) % 2
    pairs = [(index, index ^ stride) for index in range(size)]
    mine = lax.dynamic_index_in_dim(partial, digit, 0, keepdims=False)
    other = lax.dynamic_index_in_dim(partial, 1 - digit, 0, keepdims=False)
    return mine.astype(jnp.float32) + lax.ppermute(other.astype(link_dtype), axis_name, pairs).astype(jnp.float32)


def digit_of(axis_name, stride, digits):
    return (lax.axis_index(axis_name) // stride) % digits


def pair_gather(block, axis_name, stride):
    size = lax.axis_size(axis_name)
    other = lax.ppermute(block, axis_name, [(index, index ^ stride) for index in range(size)])
    first = digit_of(axis_name, stride, 2) == 0
    return jnp.stack([jnp.where(first, block, other), jnp.where(first, other, block)])


def ring_gather(block, axis_name, stride):
    size = lax.axis_size(axis_name)
    rightward = ring_step_pairs(size, stride, 4, 1)
    leftward = ring_step_pairs(size, stride, 4, -1)
    half = block.shape[0] // 2
    from_left = lax.ppermute(block, axis_name, rightward)
    from_right = lax.ppermute(block, axis_name, leftward)
    far_low = lax.ppermute(from_left[:half], axis_name, rightward)
    far_high = lax.ppermute(from_right[half:], axis_name, leftward)
    far = jnp.concatenate([far_low, far_high])
    by_offset = jnp.stack([block, from_right, far, from_left])
    return jnp.roll(by_offset, digit_of(axis_name, stride, 4), axis=0)


def line_gather(block, axis_name, stride):
    size = lax.axis_size(axis_name)
    parts = [block]
    for shift in (3, 2, 1):
        parts.append(lax.ppermute(block, axis_name, ring_step_pairs(size, stride, 4, shift)))
    return jnp.roll(jnp.stack(parts), digit_of(axis_name, stride, 4), axis=0)


def line_reduce(partial, axis_name, stride, link_dtype):
    size = lax.axis_size(axis_name)
    digit = digit_of(axis_name, stride, 4)
    total = lax.dynamic_index_in_dim(partial, digit, 0, keepdims=False).astype(jnp.float32)
    for shift in (1, 2, 3):
        outgoing = lax.dynamic_index_in_dim(partial, (digit + shift) % 4, 0, keepdims=False)
        incoming = lax.ppermute(outgoing.astype(link_dtype), axis_name, ring_step_pairs(size, stride, 4, shift))
        total = total + incoming.astype(jnp.float32)
    return total


def row_gather(block):
    rows, width = block.shape
    split = width // 2
    pair = pair_gather(block, "row", 4)
    first = jnp.swapaxes(ring_gather(pair[..., :split], "row", 1), 0, 1)
    first = ring_gather(first.reshape(8, rows, split), "row", 8).reshape(32, rows, split)
    second = ring_gather(ring_gather(pair[..., split:], "row", 8), "row", 1)
    second = jnp.transpose(second, (1, 2, 0, 3, 4)).reshape(32, rows, split)
    return jnp.concatenate([first, second], axis=-1)


def col_gather(block):
    pair = pair_gather(block, "col", 1)
    return line_gather(pair, "col", 2).reshape((8,) + block.shape)


def col_reduce(partial, link_dtype):
    core = digit_of("col", 1, 2)
    size = lax.axis_size("col")
    split = partial.reshape((4, 2) + partial.shape[1:])
    mine = lax.dynamic_index_in_dim(split, core, 1, keepdims=False).astype(jnp.float32)
    other = lax.dynamic_index_in_dim(split, 1 - core, 1, keepdims=False).astype(link_dtype)
    swapped = lax.ppermute(other, "col", [(index, index ^ 1) for index in range(size)])
    return line_reduce(mine + swapped.astype(jnp.float32), "col", 2, link_dtype)


def row_reduce(low, high, link_dtype):
    _, rows, split = low.shape
    first = low.reshape(4, 8, rows, split)
    first = ring_reduce(first, "row", 8, link_dtype).reshape(2, 4, rows, split)
    first = jnp.swapaxes(first, 0, 1)
    first = ring_reduce(first, "row", 1, link_dtype)
    second = high.reshape(4, 2, 4, rows, split)
    second = jnp.transpose(second, (2, 0, 1, 3, 4))
    second = ring_reduce(second, "row", 1, link_dtype).reshape(4, 2, rows, split)
    second = ring_reduce(second, "row", 8, link_dtype)
    both = jnp.concatenate([first, second], axis=-1)
    return pair_reduce(both, "row", 4, link_dtype)


def all_sum(terms):
    axes = ("row", "col")
    count = lax.axis_size("row") * lax.axis_size("col")
    rows, width = terms.shape
    pieces = terms.reshape(count, rows // count, width)
    spread_in = lax.all_to_all(pieces, axes, 0, 0, tiled=True)
    mine = jnp.sum(spread_in, axis=0, keepdims=True)
    spread = jnp.broadcast_to(mine, (count, rows // count, width))
    return lax.all_to_all(spread, axes, 0, 0, tiled=True).reshape(rows, width)


def layer(tile_values, tile_coords, tile_counts, features, weight_matrix, out_grad):
    values = tile_values[0, 0]
    coords = tile_coords[0, 0]
    live_count = tile_counts[0, 0]
    tile_side = values.shape[1]
    sub_rows = features.shape[2]
    width = features.shape[3]
    n_col = lax.axis_size("col")
    n_row = lax.axis_size("row")
    row_tiles = n_col * sub_rows // tile_side
    column_block = row_gather(features.reshape(sub_rows, width))
    col_source = column_block.reshape(-1, tile_side, width)
    col_tiles = col_source.shape[0]
    partial_value = tile_aggregate(
        values, coords[1], coords[0], live_count, col_source, row_tiles, False, jnp.float32
    )
    partial_value = partial_value.reshape(n_col, sub_rows, width)
    share = col_reduce(partial_value, jnp.bfloat16)
    mixed = share.astype(jnp.bfloat16).reshape(sub_rows, width)
    pre = jnp.dot(mixed, weight_matrix, preferred_element_type=jnp.float32)
    sigma = jax.nn.sigmoid(pre)
    activated = (pre * sigma).astype(jnp.bfloat16)
    pre_grad = (
        out_grad.reshape(sub_rows, width).astype(jnp.float32) * sigma * (1.0 + pre * (1.0 - sigma))
    ).astype(jnp.bfloat16)
    weight_terms = jnp.dot(mixed.T, pre_grad, preferred_element_type=jnp.float32)
    own_grad = jnp.dot(pre_grad, weight_matrix.T, preferred_element_type=jnp.float32).astype(
        jnp.bfloat16
    )
    mixed_grad = col_gather(own_grad)
    weight_grad = all_sum(weight_terms)
    row_source = mixed_grad.reshape(row_tiles, tile_side, width)
    split = width // 2
    halves = []
    for part in (row_source[..., :split], row_source[..., split:]):
        half = tile_aggregate(
            values, coords[0], coords[1], live_count, part, col_tiles, True, jnp.bfloat16
        )
        halves.append(half.reshape(n_row, sub_rows, split))
    feature_grad = row_reduce(halves[0], halves[1], jnp.bfloat16).reshape(1, 1, sub_rows, width)
    return (activated.reshape(1, 1, sub_rows, width), feature_grad, weight_grad)


def solution(mesh):
    return jax.shard_map(
        layer,
        mesh=mesh,
        in_specs=(
            P("row", "col", None, None, None),
            P("row", "col", None, None),
            P("row", "col"),
            P("col", "row", None, None),
            P(),
            P("row", "col", None, None),
        ),
        out_specs=(P("row", "col", None, None), P("col", "row", None, None), P()),
        check_vma=False,
    )
```
